256 devices in a mesh: row: 8 (over z_lo, y), col: 32 (over x, z_hi, core).
Axes of the slice: x: 4, y: 4, z: 8 (z_hi: 4, z_lo: 2; z = z_hi * 2 + z_lo), core: 2. Of those that a mesh axis runs over, the one named last changes fastest.
Arguments:
- density: bfloat16 [24576, 12288], P('row', 'col'), may hold values from -1.5 to 1.5
- neighbours: int32 [384, 192], replicated, may hold values from 0 to 383, as said below
- panels: int32 [2], replicated, may hold values from 0 to 31
Outputs:
- square_part: bfloat16 [24576, 12288], P('row', 'col')
The draws below stay inside these ranges and needn't reach their ends.
Inputs may be any that keep to these rules, and one draw needn't show every extreme that they name: In each row of neighbours, the 6 entries of every group c are distinct and lie in [c * 12, (c + 1) * 12); block row i always holds its own diagonal block i.
All inputs are finite; a program needn't handle non-finite values.
Results may differ from the reference program's by a relative error of at most 0.001.
Values may be sent and summed in bfloat16 or wider, within the bound.
No kernel may reach another device: no remote copies, remote signals or barrier semaphores. Data moves between devices by JAX's collectives and lax.ppermute only.
A program may use at most 128 MiB of HBM per device.

```python
import jax
import jax.numpy as jnp
from jax import lax

BLK = 64
CB = 12
SLOTS = 6
NB = 384
NBR = 192
ORDER = 24576
NPANEL = 32
N_COL = 32


def draw_neighbours(key, part):
    scores = jax.random.randint(key, (NB, N_COL, CB), 0, 1 << 20) * CB + jnp.arange(CB, dtype=jnp.int32)[None, None, :]
    row_ids = jnp.arange(NB, dtype=jnp.int32)
    diagonal = (row_ids[:, None, None] // CB == jnp.arange(N_COL, dtype=jnp.int32)[None, :, None]) & (row_ids[:, None, None] % CB == jnp.arange(CB, dtype=jnp.int32)[None, None, :])
    scores = jnp.where(diagonal, -1, scores)
    chosen = jnp.argsort(scores, axis=2, stable=True)[:, :, :SLOTS]
    chosen = chosen + (jnp.arange(N_COL, dtype=jnp.int32) * CB)[None, :, None]
    return chosen.reshape(NB, N_COL * SLOTS).astype(jnp.int32)


def steps_of(own_key, dims, split, low, high):
    loudness = 1.0
    for position, shards_of in split:
        steps = jax.random.uniform(jax.random.fold_in(jax.random.fold_in(own_key, 6), position), (shards_of,), jnp.float32, low / len(split), high / len(split))
        loudness = loudness * jnp.repeat(jnp.exp(steps), dims[position] // shards_of).reshape((-1,) + (1,) * (len(dims) - 1 - position))
    return loudness


def noise(stream_key, dims, deviation, most, split=(), kind=jnp.bfloat16):
    entries = jax.random.normal(stream_key, dims, jnp.float32) * deviation
    if len(split) > 0:
        entries = steps_of(stream_key, dims, split, -0.22, 0.18) * entries
    return jnp.clip(entries, min=-most, max=most).astype(kind)


def setup_inputs(seed: int = 0) -> dict:
    key_list = jax.random.split(jax.random.key(seed), 4)
    density = noise(key_list[0], (ORDER, NBR * BLK), 0.25, 1.5, ((0, 8), (1, 32)))
    neighbours = draw_neighbours(jax.random.fold_in(key_list[3], 71), 0)
    panels = jax.random.randint(key_list[2], (2,), 0, NPANEL).astype(jnp.int32)
    return dict(density=density, neighbours=neighbours, panels=panels)


def expand(values, columns, width_blocks):
    row_count = columns.shape[0]
    slot_count = columns.shape[1]
    shaped = values.reshape(row_count, BLK, slot_count, BLK).astype(jnp.float32)
    onehot = (columns[:, :, None] == jnp.arange(width_blocks, dtype=jnp.int32)[None, None, :]).astype(jnp.float32)
    dense_tile = jnp.einsum("iasb,isj->iajb", shaped, onehot)
    return dense_tile.reshape(row_count * BLK, width_blocks * BLK)


def reference(density, neighbours, panels):
    panel_width = CB * BLK
    left_list = []
    right_list = []
    for step_index in range(2):
        number = panels[step_index].astype(jnp.int32)
        group_cols = lax.dynamic_slice_in_dim(neighbours, (number * SLOTS).astype(jnp.int32), SLOTS, 1) - number * CB
        stored = lax.dynamic_slice_in_dim(density, (number * SLOTS * BLK).astype(jnp.int32), SLOTS * BLK, 1)
        left_list.append(expand(stored, group_cols, CB))
        row_band = lax.dynamic_slice_in_dim(density, (number * panel_width).astype(jnp.int32), panel_width, 0)
        band_cols = lax.dynamic_slice_in_dim(neighbours, (number * CB).astype(jnp.int32), CB, 0)
        shaped = row_band.reshape(CB, BLK, N_COL, SLOTS, BLK).astype(jnp.float32)
        local_cols = band_cols.reshape(CB, N_COL, SLOTS) - (jnp.arange(N_COL, dtype=jnp.int32) * CB)[None, :, None]
        onehot = (local_cols[:, :, :, None] == jnp.arange(CB, dtype=jnp.int32)[None, None, None, :]).astype(jnp.float32)
        dense_band = jnp.einsum("iacsb,icsj->iacjb", shaped, onehot)
        right_list.append(dense_band.reshape(panel_width, ORDER))

    def one_group(group_index):
        first_col = (group_index * panel_width).astype(jnp.int32)
        summed = jnp.zeros((ORDER, panel_width), jnp.float32)
        for step_index in range(2):
            right_piece = lax.dynamic_slice_in_dim(right_list[step_index], first_col, panel_width, 1)
            summed = summed + jnp.dot(left_list[step_index], right_piece, preferred_element_type=jnp.float32)
        rounded = lax.optimization_barrier(summed.astype(jnp.bfloat16)).astype(jnp.float32)
        rounded = rounded.reshape(NB, BLK, CB, BLK)
        local_cols = lax.dynamic_slice_in_dim(neighbours, (group_index * SLOTS).astype(jnp.int32), SLOTS, 1) - group_index * CB
        onehot = (local_cols[:, :, None] == jnp.arange(CB, dtype=jnp.int32)[None, None, :]).astype(jnp.float32)
        picked = jnp.einsum("iajb,isj->iasb", rounded, onehot)
        return picked.astype(jnp.bfloat16)

    picked_all = lax.map(one_group, jnp.arange(N_COL, dtype=jnp.int32))
    return jnp.transpose(picked_all, (1, 2, 0, 3, 4)).reshape(ORDER, NBR * BLK)
```

```python
import jax
import jax.numpy as jnp
from jax import lax
from jax.sharding import Mesh
from jax.sharding import PartitionSpec as P

BLK = 64
CB = 12
ROW_AXES = ("rz", "ry")
COL_AXES = ("cx", "cz", "cc")


def expand(values, columns, width_blocks):
    row_count, slot_count = columns.shape
    shaped = values.reshape(row_count, BLK, 1, slot_count, BLK)
    hit = columns[:, None, None, :, None] == jnp.arange(width_blocks, dtype=jnp.int32)[None, None, :, None, None]
    dense = jnp.where(hit, shaped, jnp.zeros((), values.dtype)).sum(axis=3, dtype=values.dtype)
    return dense.reshape(row_count * BLK, width_blocks * BLK)


def pick(dense, columns):
    row_count, slot_count = columns.shape
    width_blocks = dense.shape[1] // BLK
    shaped = dense.reshape(row_count, BLK, 1, width_blocks, BLK)
    hit = columns[:, None, :, None, None] == jnp.arange(width_blocks, dtype=jnp.int32)[None, None, None, :, None]
    picked = jnp.where(hit, shaped, jnp.zeros((), dense.dtype)).sum(axis=3, dtype=dense.dtype)
    return picked.reshape(row_count * BLK, slot_count * BLK)


def ring_shift(x, axis, size, step):
    return lax.ppermute(x, axis, [(i, (i + step) % size) for i in range(size)])


def row_broadcast(buf, root_z, root_y):
    z = lax.axis_index("rz")
    y = lax.axis_index("ry")
    ny = lax.axis_size("ry")
    got = ring_shift(buf, "rz", 2, 1)
    buf = jnp.where((z == root_z)[:, None, None], buf, got)
    dist = ((y - root_y + ny) % ny)[:, None, None]
    from_left = ring_shift(buf, "ry", ny, 1)
    from_right = ring_shift(buf, "ry", ny, -1)
    buf = jnp.where(dist == 1, from_left, jnp.where(dist == ny - 1, from_right, buf))
    half = buf.shape[1] // 2
    first = ring_shift(buf[:, :half], "ry", ny, 1)
    second = ring_shift(buf[:, half:], "ry", ny, -1)
    far = jnp.concatenate([first, second], axis=1)
    return jnp.where(dist == 2, far, buf)


def on_device(density, neighbours, panels):
    row_blocks = density.shape[0] // BLK
    slot_count = density.shape[1] // BLK
    col_index = (lax.axis_index("cx") * lax.axis_size("cz") + lax.axis_index("cz")) * lax.axis_size(
        "cc"
    ) + lax.axis_index("cc")
    row_index = lax.axis_index("rz") * lax.axis_size("ry") + lax.axis_index("ry")
    n_col = lax.axis_size("cx") * lax.axis_size("cz") * lax.axis_size("cc")
    panels_per_row = n_col // (lax.axis_size("rz") * lax.axis_size("ry"))
    my_rows = lax.dynamic_slice_in_dim(neighbours, row_index * row_blocks, row_blocks, 0)
    own_cols = lax.dynamic_slice_in_dim(my_rows, col_index * slot_count, slot_count, 1) - col_index * CB

    lefts = []
    bands = []
    for s in range(2):
        number = panels[s]
        lefts.append(jnp.where(col_index == number, density, jnp.zeros_like(density)))
        offset = number % panels_per_row * CB * BLK
        band = lax.dynamic_slice_in_dim(density, offset, CB * BLK, 0)
        bands.append(jnp.where(row_index == number // panels_per_row, band, jnp.zeros_like(band)))

    stacked = jnp.stack(lefts).reshape(2 * density.shape[0], density.shape[1])
    part = lax.psum_scatter(stacked, COL_AXES, scatter_dimension=0, tiled=True)
    left_all = lax.all_gather(part, COL_AXES, axis=0, tiled=True).reshape(2, *density.shape)

    band_all = jnp.stack(bands)
    owner_row = panels // panels_per_row
    n_ry = lax.axis_size("ry")
    band_all = row_broadcast(band_all, owner_row // n_ry, owner_row % n_ry)

    left_dense = []
    right_dense = []
    for s in range(2):
        number = panels[s]
        group_cols = lax.dynamic_slice_in_dim(my_rows, number * slot_count, slot_count, 1) - number * CB
        left_dense.append(expand(left_all[s], group_cols, CB))
        band_rows = lax.dynamic_slice_in_dim(neighbours, number * CB, CB, 0)
        band_cols = lax.dynamic_slice_in_dim(band_rows, col_index * slot_count, slot_count, 1) - col_index * CB
        right_dense.append(expand(band_all[s], band_cols, CB))
    summed = jnp.dot(
        jnp.concatenate(left_dense, axis=1),
        jnp.concatenate(right_dense, axis=0),
        preferred_element_type=jnp.float32,
    )
    rounded = summed.astype(jnp.bfloat16)
    return pick(rounded, own_cols)


def solution(mesh):
    n_row, n_col = mesh.devices.shape
    sub = Mesh(mesh.devices.reshape(2, n_row // 2, 4, n_col // 8, 2), ROW_AXES + COL_AXES)
    return jax.shard_map(
        on_device,
        mesh=sub,
        in_specs=(P(ROW_AXES, COL_AXES), P(), P()),
        out_specs=P(ROW_AXES, COL_AXES),
        check_vma=False,
    )
```

```python
import functools

import jax
import jax.numpy as jnp
from jax import lax
from jax.experimental import pallas as pl
from jax.experimental.pallas import tpu as pltpu
from jax.sharding import Mesh
from jax.sharding import PartitionSpec as P

BLK = 64
CB = 12
ROW_AXES = ("rz", "ry")
COL_AXES = ("cx", "cz", "cc")


def _halves(chunk):
    wide = chunk.astype(jnp.float32)
    return wide, pltpu.roll(wide, BLK, 1)


def _place_kernel(src_blocks, dst_blocks, tile_rows, block_rows, table, values, out):
    step = pl.program_id(0)
    tile = pl.program_id(1)
    lanes = lax.broadcasted_iota(jnp.int32, (BLK, 2 * BLK), 1)
    high = lanes >= BLK
    half = lanes // BLK
    placing = src_blocks < dst_blocks
    entries = src_blocks if placing else dst_blocks
    per_step = block_rows * entries
    for q in range(tile_rows // BLK):
        base = step * per_step + (tile * (tile_rows // BLK) + q) * entries
        rows = pl.ds(q * BLK, BLK)
        plain = []
        swapped = []
        for c in range(src_blocks // 2):
            a, b = _halves(values[0, rows, pl.ds(c * 2 * BLK, 2 * BLK)])
            plain.append(a)
            swapped.append(b)
        sources = []
        for t in range(src_blocks):
            own = plain[t // 2]
            other = swapped[t // 2]
            if t % 2 == 0:
                sources.append(jnp.where(high, other, own))
            else:
                sources.append(jnp.where(high, own, other))
        for p in range(dst_blocks // 2):
            acc = jnp.zeros((BLK, 2 * BLK), jnp.float32)
            for t in range(src_blocks):
                if placing:
                    hit = half + 2 * p == table[base + t]
                else:
                    hit = jnp.where(high, table[base + 2 * p + 1], table[base + 2 * p]) == t
                acc = jnp.where(hit, sources[t], acc)
            out[rows, pl.ds(p * 2 * BLK, 2 * BLK)] = acc.astype(out.dtype)


def place(values, table, src_blocks, dst_blocks, tile_rows, by_rows):
    steps, rows, _ = values.shape
    tiles = rows // tile_rows
    if not by_rows:
        out_shape = (rows, steps * dst_blocks * BLK)
        out_map = lambda s, g, tab: (g, s)
    else:
        out_shape = (steps * rows, dst_blocks * BLK)
        out_map = lambda s, g, tab: (s * tiles + g, 0)
    return pl.pallas_call(
        functools.partial(_place_kernel, src_blocks, dst_blocks, tile_rows, rows // BLK),
        out_shape=jax.ShapeDtypeStruct(out_shape, values.dtype),
        grid_spec=pltpu.PrefetchScalarGridSpec(
            num_scalar_prefetch=1,
            grid=(steps, tiles),
            in_specs=[pl.BlockSpec((1, tile_rows, src_blocks * BLK), lambda s, g, tab: (s, g, 0))],
            out_specs=pl.BlockSpec((tile_rows, dst_blocks * BLK), out_map),
        ),
    )(table, values)


def ring_shift(x, axis, size, step):
    return lax.ppermute(x, axis, [(i, (i + step) % size) for i in range(size)])


def row_broadcast(buf, root_z, root_y):
    z = lax.axis_index("rz")
    y = lax.axis_index("ry")
    ny = lax.axis_size("ry")
    got = ring_shift(buf, "rz", 2, 1)
    buf = jnp.where((z == root_z)[:, None, None], buf, got)
    dist = ((y - root_y + ny) % ny)[:, None, None]
    from_left = ring_shift(buf, "ry", ny, 1)
    from_right = ring_shift(buf, "ry", ny, -1)
    buf = jnp.where(dist == 1, from_left, jnp.where(dist == ny - 1, from_right, buf))
    half = buf.shape[1] // 2
    first = ring_shift(buf[:, :half], "ry", ny, 1)
    second = ring_shift(buf[:, half:], "ry", ny, -1)
    far = jnp.concatenate([first, second], axis=1)
    return jnp.where(dist == 2, far, buf)


def on_device(density, neighbours, panels):
    row_blocks = density.shape[0] // BLK
    slot_count = density.shape[1] // BLK
    col_index = (lax.axis_index("cx") * lax.axis_size("cz") + lax.axis_index("cz")) * lax.axis_size(
        "cc"
    ) + lax.axis_index("cc")
    row_index = lax.axis_index("rz") * lax.axis_size("ry") + lax.axis_index("ry")
    n_col = lax.axis_size("cx") * lax.axis_size("cz") * lax.axis_size("cc")
    panels_per_row = n_col // (lax.axis_size("rz") * lax.axis_size("ry"))
    my_rows = lax.dynamic_slice_in_dim(neighbours, row_index * row_blocks, row_blocks, 0)
    own_cols = lax.dynamic_slice_in_dim(my_rows, col_index * slot_count, slot_count, 1) - col_index * CB

    lefts = []
    bands = []
    for s in range(2):
        number = panels[s]
        lefts.append(jnp.where(col_index == number, density, jnp.zeros_like(density)))
        offset = number % panels_per_row * CB * BLK
        band = lax.dynamic_slice_in_dim(density, offset, CB * BLK, 0)
        bands.append(jnp.where(row_index == number // panels_per_row, band, jnp.zeros_like(band)))

    stacked = jnp.stack(lefts).reshape(2 * density.shape[0], density.shape[1])
    part = lax.psum_scatter(stacked, COL_AXES, scatter_dimension=0, tiled=True)
    left_all = lax.all_gather(part, COL_AXES, axis=0, tiled=True).reshape(2, *density.shape)

    band_all = jnp.stack(bands)
    owner_row = panels // panels_per_row
    n_ry = lax.axis_size("ry")
    band_all = row_broadcast(band_all, owner_row // n_ry, owner_row % n_ry)

    left_tables = []
    right_tables = []
    for s in range(2):
        number = panels[s]
        group_cols = lax.dynamic_slice_in_dim(my_rows, number * slot_count, slot_count, 1) - number * CB
        left_tables.append(group_cols.reshape(-1))
        band_rows = lax.dynamic_slice_in_dim(neighbours, number * CB, CB, 0)
        band_cols = lax.dynamic_slice_in_dim(band_rows, col_index * slot_count, slot_count, 1) - col_index * CB
        right_tables.append(band_cols.reshape(-1))
    left_dense = place(left_all, jnp.concatenate(left_tables), slot_count, CB, 256, False)
    right_dense = place(band_all, jnp.concatenate(right_tables), slot_count, CB, 256, True)
    product = jnp.dot(left_dense, right_dense, preferred_element_type=jnp.float32).astype(jnp.bfloat16)
    return place(product[None], own_cols.reshape(-1), CB, slot_count, 256, True)


def solution(mesh):
    n_row, n_col = mesh.devices.shape
    sub = Mesh(mesh.devices.reshape(2, n_row // 2, 4, n_col // 8, 2), ROW_AXES + COL_AXES)
    return jax.shard_map(
        on_device,
        mesh=sub,
        in_specs=(P(ROW_AXES, COL_AXES), P(), P()),
        out_specs=P(ROW_AXES, COL_AXES),
        check_vma=False,
    )
```

```python
import functools

import jax
import jax.numpy as jnp
from jax import lax
from jax.experimental import pallas as pl
from jax.experimental.pallas import tpu as pltpu
from jax.sharding import Mesh
from jax.sharding import PartitionSpec as P

BLK = 64
CB = 12
ROW_AXES = ("rz", "ry")
COL_AXES = ("cx", "cz", "cc")


def _halves(chunk):
    wide = chunk.astype(jnp.float32)
    return wide, pltpu.roll(wide, BLK, 1)


def _place_kernel(src_blocks, dst_blocks, tile_rows, block_rows, table, values, out):
    step = pl.program_id(0)
    tile = pl.program_id(1)
    lanes = lax.broadcasted_iota(jnp.int32, (BLK, 2 * BLK), 1)
    high = lanes >= BLK
    half = lanes // BLK
    placing = src_blocks < dst_blocks
    entries = src_blocks if placing else dst_blocks
    per_step = block_rows * entries
    for q in range(tile_rows // BLK):
        base = step * per_step + (tile * (tile_rows // BLK) + q) * entries
        rows = pl.ds(q * BLK, BLK)
        plain = []
        swapped = []
        for c in range(src_blocks // 2):
            a, b = _halves(values[0, rows, pl.ds(c * 2 * BLK, 2 * BLK)])
            plain.append(a)
            swapped.append(b)
        sources = []
        for t in range(src_blocks):
            own = plain[t // 2]
            other = swapped[t // 2]
            if t % 2 == 0:
                sources.append(jnp.where(high, other, own))
            else:
                sources.append(jnp.where(high, own, other))
        for p in range(dst_blocks // 2):
            acc = jnp.zeros((BLK, 2 * BLK), jnp.float32)
            for t in range(src_blocks):
                if placing:
                    hit = half + 2 * p == table[base + t]
                else:
                    hit = jnp.where(high, table[base + 2 * p + 1], table[base + 2 * p]) == t
                acc = jnp.where(hit, sources[t], acc)
            out[rows, pl.ds(p * 2 * BLK, 2 * BLK)] = acc.astype(out.dtype)


def place(values, table, src_blocks, dst_blocks, tile_rows, by_rows):
    steps, rows, _ = values.shape
    tiles = rows // tile_rows
    if not by_rows:
        out_shape = (rows, steps * dst_blocks * BLK)
        out_map = lambda s, g, tab: (g, s)
    else:
        out_shape = (steps * rows, dst_blocks * BLK)
        out_map = lambda s, g, tab: (s * tiles + g, 0)
    return pl.pallas_call(
        functools.partial(_place_kernel, src_blocks, dst_blocks, tile_rows, rows // BLK),
        out_shape=jax.ShapeDtypeStruct(out_shape, values.dtype),
        grid_spec=pltpu.PrefetchScalarGridSpec(
            num_scalar_prefetch=1,
            grid=(steps, tiles),
            in_specs=[pl.BlockSpec((1, tile_rows, src_blocks * BLK), lambda s, g, tab: (s, g, 0))],
            out_specs=pl.BlockSpec((tile_rows, dst_blocks * BLK), out_map),
        ),
    )(table, values)


def ring_shift(x, axis, size, step):
    return lax.ppermute(x, axis, [(i, (i + step) % size) for i in range(size)])


def row_broadcast(buf, root_z, root_y):
    z = lax.axis_index("rz")
    y = lax.axis_index("ry")
    ny = lax.axis_size("ry")
    got = ring_shift(buf, "rz", 2, 1)
    buf = jnp.where((z == root_z)[:, None, None], buf, got)
    dist = ((y - root_y + ny) % ny)[:, None, None]
    from_left = ring_shift(buf, "ry", ny, 1)
    from_right = ring_shift(buf, "ry", ny, -1)
    buf = jnp.where(dist == 1, from_left, jnp.where(dist == ny - 1, from_right, buf))
    half = buf.shape[1] // 2
    first = ring_shift(buf[:, :half], "ry", ny, 1)
    second = ring_shift(buf[:, half:], "ry", ny, -1)
    far = jnp.concatenate([first, second], axis=1)
    return jnp.where(dist == 2, far, buf)


def on_device(density, neighbours, panels):
    row_blocks = density.shape[0] // BLK
    slot_count = density.shape[1] // BLK
    col_index = (lax.axis_index("cx") * lax.axis_size("cz") + lax.axis_index("cz")) * lax.axis_size(
        "cc"
    ) + lax.axis_index("cc")
    row_index = lax.axis_index("rz") * lax.axis_size("ry") + lax.axis_index("ry")
    n_col = lax.axis_size("cx") * lax.axis_size("cz") * lax.axis_size("cc")
    panels_per_row = n_col // (lax.axis_size("rz") * lax.axis_size("ry"))
    my_rows = lax.dynamic_slice_in_dim(neighbours, row_index * row_blocks, row_blocks, 0)
    own_cols = lax.dynamic_slice_in_dim(my_rows, col_index * slot_count, slot_count, 1) - col_index * CB

    lefts = []
    bands = []
    for s in range(2):
        number = panels[s]
        lefts.append(jnp.where(col_index == number, density, jnp.zeros_like(density)))
        offset = number % panels_per_row * CB * BLK
        band = lax.dynamic_slice_in_dim(density, offset, CB * BLK, 0)
        bands.append(jnp.where(row_index == number // panels_per_row, band, jnp.zeros_like(band)))

    stacked = jnp.stack(lefts).reshape(2 * density.shape[0], density.shape[1])
    part = lax.psum_scatter(stacked, COL_AXES, scatter_dimension=0, tiled=True)

    band_all = jnp.stack(bands)
    owner_row = panels // panels_per_row
    n_ry = lax.axis_size("ry")
    band_all = row_broadcast(band_all, owner_row // n_ry, owner_row % n_ry)
    part, band_all = lax.optimization_barrier((part, band_all))
    left_all = lax.all_gather(part, COL_AXES, axis=0, tiled=True).reshape(2, *density.shape)

    left_tables = []
    right_tables = []
    for s in range(2):
        number = panels[s]
        group_cols = lax.dynamic_slice_in_dim(my_rows, number * slot_count, slot_count, 1) - number * CB
        left_tables.append(group_cols.reshape(-1))
        band_rows = lax.dynamic_slice_in_dim(neighbours, number * CB, CB, 0)
        band_cols = lax.dynamic_slice_in_dim(band_rows, col_index * slot_count, slot_count, 1) - col_index * CB
        right_tables.append(band_cols.reshape(-1))
    left_dense = place(left_all, jnp.concatenate(left_tables), slot_count, CB, 256, False)
    right_dense = place(band_all, jnp.concatenate(right_tables), slot_count, CB, 256, True)
    product = jnp.dot(left_dense, right_dense, preferred_element_type=jnp.float32).astype(jnp.bfloat16)
    return place(product[None], own_cols.reshape(-1), CB, slot_count, 256, True)


def solution(mesh):
    n_row, n_col = mesh.devices.shape
    sub = Mesh(mesh.devices.reshape(2, n_row // 2, 4, n_col // 8, 2), ROW_AXES + COL_AXES)
    return jax.shard_map(
        on_device,
        mesh=sub,
        in_specs=(P(ROW_AXES, COL_AXES), P(), P()),
        out_specs=P(ROW_AXES, COL_AXES),
        check_vma=False,
    )
```

```python
import functools

import jax
import jax.numpy as jnp
from jax import lax
from jax.experimental import pallas as pl
from jax.experimental.pallas import tpu as pltpu
from jax.sharding import Mesh
from jax.sharding import PartitionSpec as P

BLK = 64
CB = 12
ROW_AXES = ("rz", "ry")
COL_AXES = ("cx", "cz", "cc")


def _halves(chunk):
    return chunk, pltpu.roll(chunk, BLK, 1)


def _place_kernel(src_blocks, dst_blocks, tile_rows, block_rows, table, values, out):
    step = pl.program_id(0)
    tile = pl.program_id(1)
    lanes = lax.broadcasted_iota(jnp.int32, (BLK, 2 * BLK), 1)
    high = lanes >= BLK
    half = lanes // BLK
    placing = src_blocks < dst_blocks
    entries = src_blocks if placing else dst_blocks
    per_step = block_rows * entries

    def one_row(q, carry):
        base = step * per_step + (tile * (tile_rows // BLK) + q) * entries
        rows = pl.ds(pl.multiple_of(q * BLK, BLK), BLK)
        plain = []
        swapped = []
        for c in range(src_blocks // 2):
            a, b = _halves(values[0, rows, pl.ds(c * 2 * BLK, 2 * BLK)])
            plain.append(a)
            swapped.append(b)
        sources = []
        for t in range(src_blocks):
            own = plain[t // 2]
            other = swapped[t // 2]
            if t % 2 == 0:
                sources.append(jnp.where(high, other, own))
            else:
                sources.append(jnp.where(high, own, other))
        for p in range(dst_blocks // 2):
            acc = jnp.zeros((BLK, 2 * BLK), out.dtype)
            for t in range(src_blocks):
                if placing:
                    hit = half + 2 * p == table[base + t]
                else:
                    hit = jnp.where(high, table[base + 2 * p + 1], table[base + 2 * p]) == t
                acc = jnp.where(hit, sources[t], acc)
            out[rows, pl.ds(p * 2 * BLK, 2 * BLK)] = acc
        return carry

    lax.fori_loop(0, tile_rows // BLK, one_row, 0)


def place(values, table, src_blocks, dst_blocks, tile_rows, by_rows):
    steps, rows, _ = values.shape
    tiles = rows // tile_rows
    if not by_rows:
        out_shape = (rows, steps * dst_blocks * BLK)
        out_map = lambda s, g, tab: (g, s)
    else:
        out_shape = (steps * rows, dst_blocks * BLK)
        out_map = lambda s, g, tab: (s * tiles + g, 0)
    return pl.pallas_call(
        functools.partial(_place_kernel, src_blocks, dst_blocks, tile_rows, rows // BLK),
        out_shape=jax.ShapeDtypeStruct(out_shape, values.dtype),
        grid_spec=pltpu.PrefetchScalarGridSpec(
            num_scalar_prefetch=1,
            grid=(steps, tiles),
            in_specs=[pl.BlockSpec((1, tile_rows, src_blocks * BLK), lambda s, g, tab: (s, g, 0))],
            out_specs=pl.BlockSpec((tile_rows, dst_blocks * BLK), out_map),
        ),
    )(table, values)


def ring_shift(x, axis, size, step):
    return lax.ppermute(x, axis, [(i, (i + step) % size) for i in range(size)])


def row_broadcast(buf, root_z, root_y):
    z = lax.axis_index("rz")
    y = lax.axis_index("ry")
    ny = lax.axis_size("ry")
    got = ring_shift(buf, "rz", 2, 1)
    buf = jnp.where((z == root_z)[:, None, None], buf, got)
    dist = ((y - root_y + ny) % ny)[:, None, None]
    from_left = ring_shift(buf, "ry", ny, 1)
    from_right = ring_shift(buf, "ry", ny, -1)
    buf = jnp.where(dist == 1, from_left, jnp.where(dist == ny - 1, from_right, buf))
    half = buf.shape[1] // 2
    first = ring_shift(buf[:, :half], "ry", ny, 1)
    second = ring_shift(buf[:, half:], "ry", ny, -1)
    far = jnp.concatenate([first, second], axis=1)
    return jnp.where(dist == 2, far, buf)


def on_device(density, neighbours, panels):
    row_blocks = density.shape[0] // BLK
    slot_count = density.shape[1] // BLK
    col_index = (lax.axis_index("cx") * lax.axis_size("cz") + lax.axis_index("cz")) * lax.axis_size(
        "cc"
    ) + lax.axis_index("cc")
    row_index = lax.axis_index("rz") * lax.axis_size("ry") + lax.axis_index("ry")
    n_col = lax.axis_size("cx") * lax.axis_size("cz") * lax.axis_size("cc")
    panels_per_row = n_col // (lax.axis_size("rz") * lax.axis_size("ry"))
    my_rows = lax.dynamic_slice_in_dim(neighbours, row_index * row_blocks, row_blocks, 0)
    own_cols = lax.dynamic_slice_in_dim(my_rows, col_index * slot_count, slot_count, 1) - col_index * CB

    lefts = []
    bands = []
    for s in range(2):
        number = panels[s]
        lefts.append(jnp.where(col_index == number, density, jnp.zeros_like(density)))
        offset = number % panels_per_row * CB * BLK
        band = lax.dynamic_slice_in_dim(density, offset, CB * BLK, 0)
        bands.append(jnp.where(row_index == number // panels_per_row, band, jnp.zeros_like(band)))

    stacked = jnp.stack(lefts).reshape(2 * density.shape[0], density.shape[1])
    part = lax.psum_scatter(stacked, COL_AXES, scatter_dimension=0, tiled=True)

    band_all = jnp.stack(bands)
    owner_row = panels // panels_per_row
    n_ry = lax.axis_size("ry")
    band_all = row_broadcast(band_all, owner_row // n_ry, owner_row % n_ry)
    part, band_all = lax.optimization_barrier((part, band_all))
    left_all = lax.all_gather(part, COL_AXES, axis=0, tiled=True).reshape(2, *density.shape)

    left_tables = []
    right_tables = []
    for s in range(2):
        number = panels[s]
        group_cols = lax.dynamic_slice_in_dim(my_rows, number * slot_count, slot_count, 1) - number * CB
        left_tables.append(group_cols.reshape(-1))
        band_rows = lax.dynamic_slice_in_dim(neighbours, number * CB, CB, 0)
        band_cols = lax.dynamic_slice_in_dim(band_rows, col_index * slot_count, slot_count, 1) - col_index * CB
        right_tables.append(band_cols.reshape(-1))
    left_dense = place(left_all, jnp.concatenate(left_tables), slot_count, CB, 1536, False)
    right_dense = place(band_all, jnp.concatenate(right_tables), slot_count, CB, 768, True)
    product = jnp.dot(left_dense, right_dense, preferred_element_type=jnp.float32).astype(jnp.bfloat16)
    return place(product[None], own_cols.reshape(-1), CB, slot_count, 768, True)


def solution(mesh):
    n_row, n_col = mesh.devices.shape
    sub = Mesh(mesh.devices.reshape(2, n_row // 2, 4, n_col // 8, 2), ROW_AXES + COL_AXES)
    return jax.shard_map(
        on_device,
        mesh=sub,
        in_specs=(P(ROW_AXES, COL_AXES), P(), P()),
        out_specs=P(ROW_AXES, COL_AXES),
        check_vma=False,
    )
```

```python
import functools

import jax
import jax.numpy as jnp
from jax import lax
from jax.experimental import pallas as pl
from jax.experimental.pallas import tpu as pltpu
from jax.sharding import Mesh
from jax.sharding import PartitionSpec as P

BLK = 64
CB = 12
ROW_AXES = ("rz", "ry")
COL_AXES = ("cx", "cz", "cc")


def _halves(chunk):
    return chunk, pltpu.roll(chunk, BLK, 1)


def _place_kernel(src_blocks, dst_blocks, tile_rows, block_rows, table, values, out):
    step = pl.program_id(0)
    tile = pl.program_id(1)
    lanes = lax.broadcasted_iota(jnp.int32, (BLK, 2 * BLK), 1)
    high = lanes >= BLK
    half = lanes // BLK
    placing = src_blocks < dst_blocks
    entries = src_blocks if placing else dst_blocks
    per_step = block_rows * entries

    def one_row(q, carry):
        base = step * per_step + (tile * (tile_rows // BLK) + q) * entries
        rows = pl.ds(pl.multiple_of(q * BLK, BLK), BLK)
        plain = []
        swapped = []
        for c in range(src_blocks // 2):
            a, b = _halves(values[0, rows, pl.ds(c * 2 * BLK, 2 * BLK)])
            plain.append(a)
            swapped.append(b)
        sources = []
        for t in range(src_blocks):
            own = plain[t // 2]
            other = swapped[t // 2]
            if t % 2 == 0:
                sources.append(jnp.where(high, other, own))
            else:
                sources.append(jnp.where(high, own, other))
        for p in range(dst_blocks // 2):
            acc = jnp.zeros((BLK, 2 * BLK), out.dtype)
            for t in range(src_blocks):
                if placing:
                    hit = half + 2 * p == table[base + t]
                else:
                    hit = jnp.where(high, table[base + 2 * p + 1], table[base + 2 * p]) == t
                acc = jnp.where(hit, sources[t], acc)
            out[rows, pl.ds(p * 2 * BLK, 2 * BLK)] = acc
        return carry

    lax.fori_loop(0, tile_rows // BLK, one_row, 0)


def place(values, table, src_blocks, dst_blocks, tile_rows, by_rows):
    steps, rows, _ = values.shape
    tiles = rows // tile_rows
    if not by_rows:
        out_shape = (rows, steps * dst_blocks * BLK)
        out_map = lambda s, g, tab: (g, s)
    else:
        out_shape = (steps * rows, dst_blocks * BLK)
        out_map = lambda s, g, tab: (s * tiles + g, 0)
    return pl.pallas_call(
        functools.partial(_place_kernel, src_blocks, dst_blocks, tile_rows, rows // BLK),
        out_shape=jax.ShapeDtypeStruct(out_shape, values.dtype),
        grid_spec=pltpu.PrefetchScalarGridSpec(
            num_scalar_prefetch=1,
            grid=(steps, tiles),
            in_specs=[pl.BlockSpec((1, tile_rows, src_blocks * BLK), lambda s, g, tab: (s, g, 0))],
            out_specs=pl.BlockSpec((tile_rows, dst_blocks * BLK), out_map),
        ),
    )(table, values)


def ring_shift(x, axis, size, step):
    return lax.ppermute(x, axis, [(i, (i + step) % size) for i in range(size)])


def row_broadcast(buf, root_z, root_y):
    z = lax.axis_index("rz")
    y = lax.axis_index("ry")
    ny = lax.axis_size("ry")
    got = ring_shift(buf, "rz", 2, 1)
    buf = jnp.where((z == root_z)[:, None, None], buf, got)
    dist = ((y - root_y + ny) % ny)[:, None, None]
    from_left = ring_shift(buf, "ry", ny, 1)
    from_right = ring_shift(buf, "ry", ny, -1)
    buf = jnp.where(dist == 1, from_left, jnp.where(dist == ny - 1, from_right, buf))
    half = buf.shape[1] // 2
    first = ring_shift(buf[:, :half], "ry", ny, 1)
    second = ring_shift(buf[:, half:], "ry", ny, -1)
    far = jnp.concatenate([first, second], axis=1)
    return jnp.where(dist == 2, far, buf)


def on_device(density, neighbours, panels):
    row_blocks = density.shape[0] // BLK
    slot_count = density.shape[1] // BLK
    col_index = (lax.axis_index("cx") * lax.axis_size("cz") + lax.axis_index("cz")) * lax.axis_size(
        "cc"
    ) + lax.axis_index("cc")
    row_index = lax.axis_index("rz") * lax.axis_size("ry") + lax.axis_index("ry")
    n_col = lax.axis_size("cx") * lax.axis_size("cz") * lax.axis_size("cc")
    panels_per_row = n_col // (lax.axis_size("rz") * lax.axis_size("ry"))
    my_rows = lax.dynamic_slice_in_dim(neighbours, row_index * row_blocks, row_blocks, 0)
    own_cols = lax.dynamic_slice_in_dim(my_rows, col_index * slot_count, slot_count, 1) - col_index * CB

    core = lax.axis_index("cc")
    panels = jnp.where(core == 0, panels, panels[::-1])
    bands = []
    for s in range(2):
        number = panels[s]
        offset = number % panels_per_row * CB * BLK
        band = lax.dynamic_slice_in_dim(density, offset, CB * BLK, 0)
        bands.append(jnp.where(row_index == number // panels_per_row, band, jnp.zeros_like(band)))

    handed = ring_shift(jnp.where(col_index == panels[1], density, jnp.zeros_like(density)), "cc", 2, 1)
    carried = jnp.where(col_index == panels[0], density, handed)
    part = lax.psum_scatter(carried, ("cx", "cz"), scatter_dimension=0, tiled=True)

    band_all = jnp.stack(bands)
    owner_row = panels // panels_per_row
    n_ry = lax.axis_size("ry")
    band_all = row_broadcast(band_all, owner_row // n_ry, owner_row % n_ry)
    part, band_all = lax.optimization_barrier((part, band_all))
    mine = lax.all_gather(part, ("cx", "cz"), axis=0, tiled=True)
    other = ring_shift(mine, "cc", 2, 1)

    left_tables = []
    right_tables = []
    for s in range(2):
        number = panels[s]
        group_cols = lax.dynamic_slice_in_dim(my_rows, number * slot_count, slot_count, 1) - number * CB
        left_tables.append(group_cols.reshape(-1))
        band_rows = lax.dynamic_slice_in_dim(neighbours, number * CB, CB, 0)
        band_cols = lax.dynamic_slice_in_dim(band_rows, col_index * slot_count, slot_count, 1) - col_index * CB
        right_tables.append(band_cols.reshape(-1))
    right_dense = place(band_all, jnp.concatenate(right_tables), slot_count, CB, 768, True)
    first = place(mine[None], left_tables[0], slot_count, CB, 1536, False)
    second = place(other[None], left_tables[1], slot_count, CB, 1536, False)
    block = CB * BLK
    product = jnp.dot(first, right_dense[:block], preferred_element_type=jnp.float32)
    product = product + jnp.dot(second, right_dense[block:], preferred_element_type=jnp.float32)
    product = product.astype(jnp.bfloat16)
    return place(product[None], own_cols.reshape(-1), CB, slot_count, 768, True)


def solution(mesh):
    n_row, n_col = mesh.devices.shape
    sub = Mesh(mesh.devices.reshape(2, n_row // 2, 4, n_col // 8, 2), ROW_AXES + COL_AXES)
    return jax.shard_map(
        on_device,
        mesh=sub,
        in_specs=(P(ROW_AXES, COL_AXES), P(), P()),
        out_specs=P(ROW_AXES, COL_AXES),
        check_vma=False,
    )
```

```python
import functools

import jax
import jax.numpy as jnp
from jax import lax
from jax.experimental import pallas as pl
from jax.experimental.pallas import tpu as pltpu
from jax.sharding import Mesh
from jax.sharding import PartitionSpec as P

BLK = 64
CB = 12
ROW_AXES = ("rz", "ry")
COL_AXES = ("cx", "cz", "cc")


def _halves(chunk):
    return chunk, pltpu.roll(chunk, BLK, 1)


def _place_kernel(src_blocks, dst_blocks, tile_rows, block_rows, table, values, out):
    step = pl.program_id(0)
    tile = pl.program_id(1)
    lanes = lax.broadcasted_iota(jnp.int32, (BLK, 2 * BLK), 1)
    high = lanes >= BLK
    placing = src_blocks < dst_blocks
    entries = src_blocks if placing else dst_blocks
    per_step = block_rows * entries

    def one_row(q, carry):
        base = step * per_step + (tile * (tile_rows // BLK) + q) * entries
        rows = pl.ds(pl.multiple_of(q * BLK, BLK), BLK)
        plain = []
        swapped = []
        for c in range(src_blocks // 2):
            a, b = _halves(values[0, rows, pl.ds(c * 2 * BLK, 2 * BLK)])
            plain.append(a)
            swapped.append(b)
        low = []
        high_side = []
        for t in range(src_blocks):
            own = plain[t // 2]
            other = swapped[t // 2]
            low.append(own if t % 2 == 0 else other)
            high_side.append(other if t % 2 == 0 else own)
        for p in range(dst_blocks // 2):
            acc_low = jnp.zeros((BLK, 2 * BLK), out.dtype)
            acc_high = acc_low
            for t in range(src_blocks):
                if placing:
                    entry = table[base + t]
                    acc_low = jnp.where(entry == 2 * p, low[t], acc_low)
                    acc_high = jnp.where(entry == 2 * p + 1, high_side[t], acc_high)
                else:
                    acc_low = jnp.where(table[base + 2 * p] == t, low[t], acc_low)
                    acc_high = jnp.where(table[base + 2 * p + 1] == t, high_side[t], acc_high)
            out[rows, pl.ds(p * 2 * BLK, 2 * BLK)] = jnp.where(high, acc_high, acc_low)
        return carry

    lax.fori_loop(0, tile_rows // BLK, one_row, 0)


def place(values, table, src_blocks, dst_blocks, tile_rows, by_rows):
    steps, rows, _ = values.shape
    tiles = rows // tile_rows
    if not by_rows:
        out_shape = (rows, steps * dst_blocks * BLK)
        out_map = lambda s, g, tab: (g, s)
    else:
        out_shape = (steps * rows, dst_blocks * BLK)
        out_map = lambda s, g, tab: (s * tiles + g, 0)
    return pl.pallas_call(
        functools.partial(_place_kernel, src_blocks, dst_blocks, tile_rows, rows // BLK),
        out_shape=jax.ShapeDtypeStruct(out_shape, values.dtype),
        grid_spec=pltpu.PrefetchScalarGridSpec(
            num_scalar_prefetch=1,
            grid=(steps, tiles),
            in_specs=[pl.BlockSpec((1, tile_rows, src_blocks * BLK), lambda s, g, tab: (s, g, 0))],
            out_specs=pl.BlockSpec((tile_rows, dst_blocks * BLK), out_map),
        ),
    )(table, values)


def ring_shift(x, axis, size, step):
    return lax.ppermute(x, axis, [(i, (i + step) % size) for i in range(size)])


def row_broadcast(buf, root_z, root_y):
    z = lax.axis_index("rz")
    y = lax.axis_index("ry")
    ny = lax.axis_size("ry")
    got = ring_shift(buf, "rz", 2, 1)
    buf = jnp.where((z == root_z)[:, None, None], buf, got)
    dist = ((y - root_y + ny) % ny)[:, None, None]
    from_left = ring_shift(buf, "ry", ny, 1)
    from_right = ring_shift(buf, "ry", ny, -1)
    buf = jnp.where(dist == 1, from_left, jnp.where(dist == ny - 1, from_right, buf))
    half = buf.shape[1] // 2
    first = ring_shift(buf[:, :half], "ry", ny, 1)
    second = ring_shift(buf[:, half:], "ry", ny, -1)
    far = jnp.concatenate([first, second], axis=1)
    return jnp.where(dist == 2, far, buf)


def on_device(density, neighbours, panels):
    row_blocks = density.shape[0] // BLK
    slot_count = density.shape[1] // BLK
    col_index = (lax.axis_index("cx") * lax.axis_size("cz") + lax.axis_index("cz")) * lax.axis_size(
        "cc"
    ) + lax.axis_index("cc")
    row_index = lax.axis_index("rz") * lax.axis_size("ry") + lax.axis_index("ry")
    n_col = lax.axis_size("cx") * lax.axis_size("cz") * lax.axis_size("cc")
    panels_per_row = n_col // (lax.axis_size("rz") * lax.axis_size("ry"))
    my_rows = lax.dynamic_slice_in_dim(neighbours, row_index * row_blocks, row_blocks, 0)
    own_cols = lax.dynamic_slice_in_dim(my_rows, col_index * slot_count, slot_count, 1) - col_index * CB

    lefts = []
    bands = []
    for s in range(2):
        number = panels[s]
        lefts.append(jnp.where(col_index == number, density, jnp.zeros_like(density)))
        offset = number % panels_per_row * CB * BLK
        band = lax.dynamic_slice_in_dim(density, offset, CB * BLK, 0)
        bands.append(jnp.where(row_index == number // panels_per_row, band, jnp.zeros_like(band)))

    stacked = jnp.stack(lefts).reshape(2 * density.shape[0], density.shape[1])
    part = lax.psum_scatter(stacked, COL_AXES, scatter_dimension=0, tiled=True)

    band_all = jnp.stack(bands)
    owner_row = panels // panels_per_row
    n_ry = lax.axis_size("ry")
    band_all = row_broadcast(band_all, owner_row // n_ry, owner_row % n_ry)
    part, band_all = lax.optimization_barrier((part, band_all))
    left_all = lax.all_gather(part, COL_AXES, axis=0, tiled=True).reshape(2, *density.shape)

    left_tables = []
    right_tables = []
    for s in range(2):
        number = panels[s]
        group_cols = lax.dynamic_slice_in_dim(my_rows, number * slot_count, slot_count, 1) - number * CB
        left_tables.append(group_cols.reshape(-1))
        band_rows = lax.dynamic_slice_in_dim(neighbours, number * CB, CB, 0)
        band_cols = lax.dynamic_slice_in_dim(band_rows, col_index * slot_count, slot_count, 1) - col_index * CB
        right_tables.append(band_cols.reshape(-1))
    left_dense = place(left_all, jnp.concatenate(left_tables), slot_count, CB, 1536, False)
    right_dense = place(band_all, jnp.concatenate(right_tables), slot_count, CB, 768, True)
    product = jnp.dot(left_dense, right_dense, preferred_element_type=jnp.float32).astype(jnp.bfloat16)
    return place(product[None], own_cols.reshape(-1), CB, slot_count, 768, True)


def solution(mesh):
    n_row, n_col = mesh.devices.shape
    sub = Mesh(mesh.devices.reshape(2, n_row // 2, 4, n_col // 8, 2), ROW_AXES + COL_AXES)
    return jax.shard_map(
        on_device,
        mesh=sub,
        in_specs=(P(ROW_AXES, COL_AXES), P(), P()),
        out_specs=P(ROW_AXES, COL_AXES),
        check_vma=False,
    )
```

```python
import functools

import jax
import jax.numpy as jnp
from jax import lax
from jax.experimental import pallas as pl
from jax.experimental.pallas import tpu as pltpu
from jax.sharding import Mesh
from jax.sharding import PartitionSpec as P

BLK = 64
CB = 12
ROW_AXES = ("rz", "ry")
COL_AXES = ("cx", "cz", "cc")


def _halves(chunk):
    return chunk, pltpu.roll(chunk, BLK, 1)


def _place_kernel(src_blocks, dst_blocks, tile_rows, block_rows, table, values, out):
    step = pl.program_id(0)
    tile = pl.program_id(1)
    lanes = lax.broadcasted_iota(jnp.int32, (BLK, 2 * BLK), 1)
    high = lanes >= BLK
    half = lanes // BLK
    placing = src_blocks < dst_blocks
    entries = src_blocks if placing else dst_blocks
    per_step = block_rows * entries

    def one_row(q, carry):
        base = step * per_step + (tile * (tile_rows // BLK) + q) * entries
        rows = pl.ds(pl.multiple_of(q * BLK, BLK), BLK)
        plain = []
        swapped = []
        for c in range(src_blocks // 2):
            a, b = _halves(values[0, rows, pl.ds(c * 2 * BLK, 2 * BLK)])
            plain.append(a)
            swapped.append(b)
        sources = []
        for t in range(src_blocks):
            own = plain[t // 2]
            other = swapped[t // 2]
            if t % 2 == 0:
                sources.append(jnp.where(high, other, own))
            else:
                sources.append(jnp.where(high, own, other))
        for p in range(dst_blocks // 2):
            acc = jnp.zeros((BLK, 2 * BLK), out.dtype)
            for t in range(src_blocks):
                if placing:
                    hit = half + 2 * p == table[base + t]
                else:
                    hit = jnp.where(high, table[base + 2 * p + 1], table[base + 2 * p]) == t
                acc = jnp.where(hit, sources[t], acc)
            out[rows, pl.ds(p * 2 * BLK, 2 * BLK)] = acc
        return carry

    lax.fori_loop(0, tile_rows // BLK, one_row, 0)


def place(values, table, src_blocks, dst_blocks, tile_rows, by_rows):
    steps, rows, _ = values.shape
    tiles = rows // tile_rows
    if not by_rows:
        out_shape = (rows, steps * dst_blocks * BLK)
        out_map = lambda s, g, tab: (g, s)
    else:
        out_shape = (steps * rows, dst_blocks * BLK)
        out_map = lambda s, g, tab: (s * tiles + g, 0)
    return pl.pallas_call(
        functools.partial(_place_kernel, src_blocks, dst_blocks, tile_rows, rows // BLK),
        out_shape=jax.ShapeDtypeStruct(out_shape, values.dtype),
        grid_spec=pltpu.PrefetchScalarGridSpec(
            num_scalar_prefetch=1,
            grid=(steps, tiles),
            in_specs=[pl.BlockSpec((1, tile_rows, src_blocks * BLK), lambda s, g, tab: (s, g, 0))],
            out_specs=pl.BlockSpec((tile_rows, dst_blocks * BLK), out_map),
        ),
    )(table, values)


def ring_shift(x, axis, size, step):
    return lax.ppermute(x, axis, [(i, (i + step) % size) for i in range(size)])


def row_broadcast(buf, root_z, root_y):
    z = lax.axis_index("rz")
    y = lax.axis_index("ry")
    ny = lax.axis_size("ry")
    got = ring_shift(buf, "rz", 2, 1)
    buf = jnp.where((z == root_z)[:, None, None], buf, got)
    dist = ((y - root_y + ny) % ny)[:, None, None]
    from_left = ring_shift(buf, "ry", ny, 1)
    from_right = ring_shift(buf, "ry", ny, -1)
    buf = jnp.where(dist == 1, from_left, jnp.where(dist == ny - 1, from_right, buf))
    half = buf.shape[1] // 2
    first = ring_shift(buf[:, :half], "ry", ny, 1)
    second = ring_shift(buf[:, half:], "ry", ny, -1)
    far = jnp.concatenate([first, second], axis=1)
    return jnp.where(dist == 2, far, buf)


def on_device(density, neighbours, panels):
    row_blocks = density.shape[0] // BLK
    slot_count = density.shape[1] // BLK
    col_index = (lax.axis_index("cx") * lax.axis_size("cz") + lax.axis_index("cz")) * lax.axis_size(
        "cc"
    ) + lax.axis_index("cc")
    row_index = lax.axis_index("rz") * lax.axis_size("ry") + lax.axis_index("ry")
    n_col = lax.axis_size("cx") * lax.axis_size("cz") * lax.axis_size("cc")
    panels_per_row = n_col // (lax.axis_size("rz") * lax.axis_size("ry"))
    my_rows = lax.dynamic_slice_in_dim(neighbours, row_index * row_blocks, row_blocks, 0)
    own_cols = lax.dynamic_slice_in_dim(my_rows, col_index * slot_count, slot_count, 1) - col_index * CB

    own_dense = place(density[None], own_cols.reshape(-1), slot_count, CB, 1536, False)
    lefts = []
    bands = []
    for s in range(2):
        number = panels[s]
        lefts.append(jnp.where(col_index == number, own_dense, jnp.zeros_like(own_dense)))
        offset = number % panels_per_row * CB * BLK
        band = lax.dynamic_slice_in_dim(density, offset, CB * BLK, 0)
        bands.append(jnp.where(row_index == number // panels_per_row, band, jnp.zeros_like(band)))

    stacked = jnp.stack(lefts).reshape(2 * own_dense.shape[0], own_dense.shape[1])
    part = lax.psum_scatter(stacked, COL_AXES, scatter_dimension=0, tiled=True)

    band_all = jnp.stack(bands)
    owner_row = panels // panels_per_row
    n_ry = lax.axis_size("ry")
    band_all = row_broadcast(band_all, owner_row // n_ry, owner_row % n_ry)
    part, band_all = lax.optimization_barrier((part, band_all))
    left_all = lax.all_gather(part, COL_AXES, axis=0, tiled=True).reshape(2, *own_dense.shape)

    right_tables = []
    for s in range(2):
        number = panels[s]
        band_rows = lax.dynamic_slice_in_dim(neighbours, number * CB, CB, 0)
        band_cols = lax.dynamic_slice_in_dim(band_rows, col_index * slot_count, slot_count, 1) - col_index * CB
        right_tables.append(band_cols.reshape(-1))
    right_dense = place(band_all, jnp.concatenate(right_tables), slot_count, CB, 768, True)
    right_dense = right_dense.reshape(2, CB * BLK, CB * BLK)
    product = jnp.einsum("sik,skj->ij", left_all, right_dense, preferred_element_type=jnp.float32)
    product = product.astype(jnp.bfloat16)
    return place(product[None], own_cols.reshape(-1), CB, slot_count, 768, True)


def solution(mesh):
    n_row, n_col = mesh.devices.shape
    sub = Mesh(mesh.devices.reshape(2, n_row // 2, 4, n_col // 8, 2), ROW_AXES + COL_AXES)
    return jax.shard_map(
        on_device,
        mesh=sub,
        in_specs=(P(ROW_AXES, COL_AXES), P(), P()),
        out_specs=P(ROW_AXES, COL_AXES),
        check_vma=False,
    )
```

```python
import functools

import jax
import jax.numpy as jnp
from jax import lax
from jax.experimental import pallas as pl
from jax.experimental.pallas import tpu as pltpu
from jax.sharding import Mesh
from jax.sharding import PartitionSpec as P

BLK = 64
CB = 12
ROW_AXES = ("rz", "ry")
COL_AXES = ("cx", "cz", "cc")


def _halves(chunk):
    return chunk, pltpu.roll(chunk, BLK, 1)


def _place_kernel(src_blocks, dst_blocks, tile_rows, block_rows, table, values, out):
    step = pl.program_id(0)
    tile = pl.program_id(1)
    lanes = lax.broadcasted_iota(jnp.int32, (BLK, 2 * BLK), 1)
    high = lanes >= BLK
    half = lanes // BLK
    placing = src_blocks < dst_blocks
    entries = src_blocks if placing else dst_blocks
    per_step = block_rows * entries

    def one_row(q, carry):
        base = step * per_step + (tile * (tile_rows // BLK) + q) * entries
        rows = pl.ds(pl.multiple_of(q * BLK, BLK), BLK)
        plain = []
        swapped = []
        for c in range(src_blocks // 2):
            a, b = _halves(values[0, rows, pl.ds(c * 2 * BLK, 2 * BLK)])
            plain.append(a)
            swapped.append(b)
        sources = []
        for t in range(src_blocks):
            own = plain[t // 2]
            other = swapped[t // 2]
            if t % 2 == 0:
                sources.append(jnp.where(high, other, own))
            else:
                sources.append(jnp.where(high, own, other))
        for p in range(dst_blocks // 2):
            acc = jnp.zeros((BLK, 2 * BLK), out.dtype)
            for t in range(src_blocks):
                if placing:
                    hit = half + 2 * p == table[base + t]
                else:
                    hit = jnp.where(high, table[base + 2 * p + 1], table[base + 2 * p]) == t
                acc = jnp.where(hit, sources[t], acc)
            out[rows, pl.ds(p * 2 * BLK, 2 * BLK)] = acc
        return carry

    lax.fori_loop(0, tile_rows // BLK, one_row, 0)


def place(values, table, src_blocks, dst_blocks, tile_rows, by_rows):
    steps, rows, _ = values.shape
    tiles = rows // tile_rows
    if not by_rows:
        out_shape = (rows, steps * dst_blocks * BLK)
        out_map = lambda s, g, tab: (g, s)
    else:
        out_shape = (steps * rows, dst_blocks * BLK)
        out_map = lambda s, g, tab: (s * tiles + g, 0)
    return pl.pallas_call(
        functools.partial(_place_kernel, src_blocks, dst_blocks, tile_rows, rows // BLK),
        out_shape=jax.ShapeDtypeStruct(out_shape, values.dtype),
        grid_spec=pltpu.PrefetchScalarGridSpec(
            num_scalar_prefetch=1,
            grid=(steps, tiles),
            in_specs=[pl.BlockSpec((1, tile_rows, src_blocks * BLK), lambda s, g, tab: (s, g, 0))],
            out_specs=pl.BlockSpec((tile_rows, dst_blocks * BLK), out_map),
        ),
    )(table, values)


def ring_shift(x, axis, size, step):
    return lax.ppermute(x, axis, [(i, (i + step) % size) for i in range(size)])


def row_broadcast(buf, root_z, root_y):
    z = lax.axis_index("rz")
    y = lax.axis_index("ry")
    ny = lax.axis_size("ry")
    got = ring_shift(buf, "rz", 2, 1)
    buf = jnp.where((z == root_z)[:, None, None], buf, got)
    dist = ((y - root_y + ny) % ny)[:, None, None]
    from_left = ring_shift(buf, "ry", ny, 1)
    from_right = ring_shift(buf, "ry", ny, -1)
    buf = jnp.where(dist == 1, from_left, jnp.where(dist == ny - 1, from_right, buf))
    half = buf.shape[1] // 2
    first = ring_shift(buf[:, :half], "ry", ny, 1)
    second = ring_shift(buf[:, half:], "ry", ny, -1)
    far = jnp.concatenate([first, second], axis=1)
    return jnp.where(dist == 2, far, buf)


def on_device(density, neighbours, panels):
    row_blocks = density.shape[0] // BLK
    slot_count = density.shape[1] // BLK
    col_index = (lax.axis_index("cx") * lax.axis_size("cz") + lax.axis_index("cz")) * lax.axis_size(
        "cc"
    ) + lax.axis_index("cc")
    row_index = lax.axis_index("rz") * lax.axis_size("ry") + lax.axis_index("ry")
    n_col = lax.axis_size("cx") * lax.axis_size("cz") * lax.axis_size("cc")
    panels_per_row = n_col // (lax.axis_size("rz") * lax.axis_size("ry"))
    my_rows = lax.dynamic_slice_in_dim(neighbours, row_index * row_blocks, row_blocks, 0)
    own_cols = lax.dynamic_slice_in_dim(my_rows, col_index * slot_count, slot_count, 1) - col_index * CB

    roots = (col_index == panels)[:, None, None]
    stacked = jnp.where(roots, density[None], jnp.zeros((), density.dtype))
    bands = []
    for s in range(2):
        number = panels[s]
        offset = number % panels_per_row * CB * BLK
        band = lax.dynamic_slice_in_dim(density, offset, CB * BLK, 0)
        bands.append(jnp.where(row_index == number // panels_per_row, band, jnp.zeros_like(band)))

    stacked = stacked.reshape(2 * density.shape[0], density.shape[1])
    part = lax.psum_scatter(stacked, COL_AXES, scatter_dimension=0, tiled=True)

    band_all = jnp.stack(bands)
    owner_row = panels // panels_per_row
    n_ry = lax.axis_size("ry")
    band_all = row_broadcast(band_all, owner_row // n_ry, owner_row % n_ry)
    part, band_all = lax.optimization_barrier((part, band_all))
    left_all = lax.all_gather(part, COL_AXES, axis=0, tiled=True).reshape(2, *density.shape)

    left_tables = []
    right_tables = []
    for s in range(2):
        number = panels[s]
        group_cols = lax.dynamic_slice_in_dim(my_rows, number * slot_count, slot_count, 1) - number * CB
        left_tables.append(group_cols.reshape(-1))
        band_rows = lax.dynamic_slice_in_dim(neighbours, number * CB, CB, 0)
        band_cols = lax.dynamic_slice_in_dim(band_rows, col_index * slot_count, slot_count, 1) - col_index * CB
        right_tables.append(band_cols.reshape(-1))
    left_dense = place(left_all, jnp.concatenate(left_tables), slot_count, CB, 1536, False)
    right_dense = place(band_all, jnp.concatenate(right_tables), slot_count, CB, 768, True)
    product = jnp.dot(left_dense, right_dense, preferred_element_type=jnp.float32).astype(jnp.bfloat16)
    return place(product[None], own_cols.reshape(-1), CB, slot_count, 768, True)


def solution(mesh):
    n_row, n_col = mesh.devices.shape
    sub = Mesh(mesh.devices.reshape(2, n_row // 2, 4, n_col // 8, 2), ROW_AXES + COL_AXES)
    return jax.shard_map(
        on_device,
        mesh=sub,
        in_specs=(P(ROW_AXES, COL_AXES), P(), P()),
        out_specs=P(ROW_AXES, COL_AXES),
        check_vma=False,
    )
```

```python
import functools

import jax
import jax.numpy as jnp
from jax import lax
from jax.experimental import pallas as pl
from jax.experimental.pallas import tpu as pltpu
from jax.sharding import Mesh
from jax.sharding import PartitionSpec as P

BLK = 64
CB = 12
ROW_AXES = ("rz", "ry")
COL_AXES = ("cx", "cz", "cc")


def _halves(chunk):
    return chunk, pltpu.roll(chunk, BLK, 1)


def _place_kernel(src_blocks, dst_blocks, tile_rows, block_rows, table, values, out):
    step = pl.program_id(0)
    tile = pl.program_id(1)
    lanes = lax.broadcasted_iota(jnp.int32, (BLK, 2 * BLK), 1)
    high = lanes >= BLK
    half = lanes // BLK
    placing = src_blocks < dst_blocks
    entries = src_blocks if placing else dst_blocks
    per_step = block_rows * entries

    def one_row(q, carry):
        base = step * per_step + (tile * (tile_rows // BLK) + q) * entries
        rows = pl.ds(pl.multiple_of(q * BLK, BLK), BLK)
        plain = []
        swapped = []
        for c in range(src_blocks // 2):
            a, b = _halves(values[0, rows, pl.ds(c * 2 * BLK, 2 * BLK)])
            plain.append(a)
            swapped.append(b)
        sources = []
        for t in range(src_blocks):
            own = plain[t // 2]
            other = swapped[t // 2]
            if t % 2 == 0:
                sources.append(jnp.where(high, other, own))
            else:
                sources.append(jnp.where(high, own, other))
        for p in range(dst_blocks // 2):
            acc = jnp.zeros((BLK, 2 * BLK), out.dtype)
            for t in range(src_blocks):
                if placing:
                    hit = half + 2 * p == table[base + t]
                else:
                    hit = jnp.where(high, table[base + 2 * p + 1], table[base + 2 * p]) == t
                acc = jnp.where(hit, sources[t], acc)
            out[rows, pl.ds(p * 2 * BLK, 2 * BLK)] = acc
        return carry

    lax.fori_loop(0, tile_rows // BLK, one_row, 0)


def _product_pick_kernel(tile_rows, block_rows, table, left, right, out, product):
    product[0] = jnp.dot(left[...], right[...], preferred_element_type=jnp.float32).astype(product.dtype)
    _place_kernel(CB, out.shape[1] // BLK, tile_rows, block_rows, table, product, out)


def product_pick(left, right, table, tile_rows):
    rows = left.shape[0]
    width = right.shape[1]
    slots = table.shape[0] // (rows // BLK)
    return pl.pallas_call(
        functools.partial(_product_pick_kernel, tile_rows, rows // BLK),
        out_shape=jax.ShapeDtypeStruct((rows, slots * BLK), left.dtype),
        grid_spec=pltpu.PrefetchScalarGridSpec(
            num_scalar_prefetch=1,
            grid=(1, rows // tile_rows),
            in_specs=[
                pl.BlockSpec((tile_rows, left.shape[1]), lambda s, g, tab: (g, 0)),
                pl.BlockSpec(right.shape, lambda s, g, tab: (0, 0)),
            ],
            out_specs=pl.BlockSpec((tile_rows, slots * BLK), lambda s, g, tab: (g, 0)),
            scratch_shapes=[pltpu.VMEM((1, tile_rows, width), left.dtype)],
        ),
    )(table, left, right)


def place(values, table, src_blocks, dst_blocks, tile_rows, by_rows):
    steps, rows, _ = values.shape
    tiles = rows // tile_rows
    if not by_rows:
        out_shape = (rows, steps * dst_blocks * BLK)
        out_map = lambda s, g, tab: (g, s)
    else:
        out_shape = (steps * rows, dst_blocks * BLK)
        out_map = lambda s, g, tab: (s * tiles + g, 0)
    return pl.pallas_call(
        functools.partial(_place_kernel, src_blocks, dst_blocks, tile_rows, rows // BLK),
        out_shape=jax.ShapeDtypeStruct(out_shape, values.dtype),
        grid_spec=pltpu.PrefetchScalarGridSpec(
            num_scalar_prefetch=1,
            grid=(steps, tiles),
            in_specs=[pl.BlockSpec((1, tile_rows, src_blocks * BLK), lambda s, g, tab: (s, g, 0))],
            out_specs=pl.BlockSpec((tile_rows, dst_blocks * BLK), out_map),
        ),
    )(table, values)


def ring_shift(x, axis, size, step):
    return lax.ppermute(x, axis, [(i, (i + step) % size) for i in range(size)])


def row_broadcast(buf, root_z, root_y):
    z = lax.axis_index("rz")
    y = lax.axis_index("ry")
    ny = lax.axis_size("ry")
    got = ring_shift(buf, "rz", 2, 1)
    buf = jnp.where((z == root_z)[:, None, None], buf, got)
    dist = ((y - root_y + ny) % ny)[:, None, None]
    from_left = ring_shift(buf, "ry", ny, 1)
    from_right = ring_shift(buf, "ry", ny, -1)
    buf = jnp.where(dist == 1, from_left, jnp.where(dist == ny - 1, from_right, buf))
    half = buf.shape[1] // 2
    first = ring_shift(buf[:, :half], "ry", ny, 1)
    second = ring_shift(buf[:, half:], "ry", ny, -1)
    far = jnp.concatenate([first, second], axis=1)
    return jnp.where(dist == 2, far, buf)


def on_device(density, neighbours, panels):
    row_blocks = density.shape[0] // BLK
    slot_count = density.shape[1] // BLK
    col_index = (lax.axis_index("cx") * lax.axis_size("cz") + lax.axis_index("cz")) * lax.axis_size(
        "cc"
    ) + lax.axis_index("cc")
    row_index = lax.axis_index("rz") * lax.axis_size("ry") + lax.axis_index("ry")
    n_col = lax.axis_size("cx") * lax.axis_size("cz") * lax.axis_size("cc")
    panels_per_row = n_col // (lax.axis_size("rz") * lax.axis_size("ry"))
    my_rows = lax.dynamic_slice_in_dim(neighbours, row_index * row_blocks, row_blocks, 0)
    own_cols = lax.dynamic_slice_in_dim(my_rows, col_index * slot_count, slot_count, 1) - col_index * CB

    roots = (col_index == panels)[:, None, None]
    stacked = jnp.where(roots, density[None], jnp.zeros((), density.dtype))
    bands = []
    for s in range(2):
        number = panels[s]
        offset = number % panels_per_row * CB * BLK
        band = lax.dynamic_slice_in_dim(density, offset, CB * BLK, 0)
        bands.append(jnp.where(row_index == number // panels_per_row, band, jnp.zeros_like(band)))

    stacked = stacked.reshape(2 * density.shape[0], density.shape[1])
    part = lax.psum_scatter(stacked, COL_AXES, scatter_dimension=0, tiled=True)

    band_all = jnp.stack(bands)
    owner_row = panels // panels_per_row
    n_ry = lax.axis_size("ry")
    band_all = row_broadcast(band_all, owner_row // n_ry, owner_row % n_ry)
    part, band_all = lax.optimization_barrier((part, band_all))
    left_all = lax.all_gather(part, COL_AXES, axis=0, tiled=True).reshape(2, *density.shape)

    left_tables = []
    right_tables = []
    for s in range(2):
        number = panels[s]
        group_cols = lax.dynamic_slice_in_dim(my_rows, number * slot_count, slot_count, 1) - number * CB
        left_tables.append(group_cols.reshape(-1))
        band_rows = lax.dynamic_slice_in_dim(neighbours, number * CB, CB, 0)
        band_cols = lax.dynamic_slice_in_dim(band_rows, col_index * slot_count, slot_count, 1) - col_index * CB
        right_tables.append(band_cols.reshape(-1))
    left_dense = place(left_all, jnp.concatenate(left_tables), slot_count, CB, 1536, False)
    right_dense = place(band_all, jnp.concatenate(right_tables), slot_count, CB, 768, True)
    return product_pick(left_dense, right_dense, own_cols.reshape(-1), 256)


def solution(mesh):
    n_row, n_col = mesh.devices.shape
    sub = Mesh(mesh.devices.reshape(2, n_row // 2, 4, n_col // 8, 2), ROW_AXES + COL_AXES)
    return jax.shard_map(
        on_device,
        mesh=sub,
        in_specs=(P(ROW_AXES, COL_AXES), P(), P()),
        out_specs=P(ROW_AXES, COL_AXES),
        check_vma=False,
    )
```

```python
import functools

import jax
import jax.numpy as jnp
from jax import lax
from jax.experimental import pallas as pl
from jax.experimental.pallas import tpu as pltpu
from jax.sharding import Mesh
from jax.sharding import PartitionSpec as P

BLK = 64
CB = 12
ROW_AXES = ("rz", "ry")
COL_AXES = ("cx", "cz", "cc")


def _halves(chunk):
    return chunk, pltpu.roll(chunk, BLK, 1)


def _place_kernel(src_blocks, dst_blocks, tile_rows, block_rows, table, values, out):
    _place_body(src_blocks, dst_blocks, tile_rows, block_rows, table, values, out, pl.program_id(0), pl.program_id(1), 0)


def _place_body(src_blocks, dst_blocks, tile_rows, block_rows, table, values, out, step, tile, offset):
    lanes = lax.broadcasted_iota(jnp.int32, (BLK, 2 * BLK), 1)
    high = lanes >= BLK
    half = lanes // BLK
    placing = src_blocks < dst_blocks
    entries = src_blocks if placing else dst_blocks
    per_step = block_rows * entries

    def one_row(q, carry):
        base = offset + step * per_step + (tile * (tile_rows // BLK) + q) * entries
        rows = pl.ds(pl.multiple_of(q * BLK, BLK), BLK)
        plain = []
        swapped = []
        for c in range(src_blocks // 2):
            a, b = _halves(values[0, rows, pl.ds(c * 2 * BLK, 2 * BLK)])
            plain.append(a)
            swapped.append(b)
        sources = []
        for t in range(src_blocks):
            own = plain[t // 2]
            other = swapped[t // 2]
            if t % 2 == 0:
                sources.append(jnp.where(high, other, own))
            else:
                sources.append(jnp.where(high, own, other))
        for p in range(dst_blocks // 2):
            acc = jnp.zeros((BLK, 2 * BLK), out.dtype)
            for t in range(src_blocks):
                if placing:
                    hit = half + 2 * p == table[base + t]
                else:
                    hit = jnp.where(high, table[base + 2 * p + 1], table[base + 2 * p]) == t
                acc = jnp.where(hit, sources[t], acc)
            out[rows, pl.ds(p * 2 * BLK, 2 * BLK)] = acc
        return carry

    lax.fori_loop(0, tile_rows // BLK, one_row, 0)


def _fused_kernel(tile_rows, block_rows, slots, table, left, right, out, dense, product):
    tile = pl.program_id(1)
    steps = left.shape[0]
    width = CB * BLK
    for s in range(steps):
        view = dense.at[:, pl.ds(s * width, width)]
        _place_body(slots, CB, tile_rows, block_rows, table, left.at[pl.ds(s, 1)], view, s, tile, 0)
    product[0] = jnp.dot(dense[...], right[...], preferred_element_type=jnp.float32).astype(product.dtype)
    _place_body(CB, slots, tile_rows, block_rows, table, product, out, 0, tile, steps * block_rows * slots)


def fused_product(left, right, table, slots, tile_rows):
    steps, rows, _ = left.shape
    return pl.pallas_call(
        functools.partial(_fused_kernel, tile_rows, rows // BLK, slots),
        out_shape=jax.ShapeDtypeStruct((rows, slots * BLK), left.dtype),
        grid_spec=pltpu.PrefetchScalarGridSpec(
            num_scalar_prefetch=1,
            grid=(1, rows // tile_rows),
            in_specs=[
                pl.BlockSpec((steps, tile_rows, left.shape[2]), lambda s, g, tab: (0, g, 0)),
                pl.BlockSpec(right.shape, lambda s, g, tab: (0, 0)),
            ],
            out_specs=pl.BlockSpec((tile_rows, slots * BLK), lambda s, g, tab: (g, 0)),
            scratch_shapes=[
                pltpu.VMEM((tile_rows, steps * CB * BLK), left.dtype),
                pltpu.VMEM((1, tile_rows, right.shape[1]), left.dtype),
            ],
        ),
    )(table, left, right)


def place(values, table, src_blocks, dst_blocks, tile_rows, by_rows):
    steps, rows, _ = values.shape
    tiles = rows // tile_rows
    if not by_rows:
        out_shape = (rows, steps * dst_blocks * BLK)
        out_map = lambda s, g, tab: (g, s)
    else:
        out_shape = (steps * rows, dst_blocks * BLK)
        out_map = lambda s, g, tab: (s * tiles + g, 0)
    return pl.pallas_call(
        functools.partial(_place_kernel, src_blocks, dst_blocks, tile_rows, rows // BLK),
        out_shape=jax.ShapeDtypeStruct(out_shape, values.dtype),
        grid_spec=pltpu.PrefetchScalarGridSpec(
            num_scalar_prefetch=1,
            grid=(steps, tiles),
            in_specs=[pl.BlockSpec((1, tile_rows, src_blocks * BLK), lambda s, g, tab: (s, g, 0))],
            out_specs=pl.BlockSpec((tile_rows, dst_blocks * BLK), out_map),
        ),
    )(table, values)


def ring_shift(x, axis, size, step):
    return lax.ppermute(x, axis, [(i, (i + step) % size) for i in range(size)])


def row_broadcast(buf, root_z, root_y):
    z = lax.axis_index("rz")
    y = lax.axis_index("ry")
    ny = lax.axis_size("ry")
    got = ring_shift(buf, "rz", 2, 1)
    buf = jnp.where((z == root_z)[:, None, None], buf, got)
    dist = ((y - root_y + ny) % ny)[:, None, None]
    from_left = ring_shift(buf, "ry", ny, 1)
    from_right = ring_shift(buf, "ry", ny, -1)
    buf = jnp.where(dist == 1, from_left, jnp.where(dist == ny - 1, from_right, buf))
    half = buf.shape[1] // 2
    first = ring_shift(buf[:, :half], "ry", ny, 1)
    second = ring_shift(buf[:, half:], "ry", ny, -1)
    far = jnp.concatenate([first, second], axis=1)
    return jnp.where(dist == 2, far, buf)


def on_device(density, neighbours, panels):
    row_blocks = density.shape[0] // BLK
    slot_count = density.shape[1] // BLK
    col_index = (lax.axis_index("cx") * lax.axis_size("cz") + lax.axis_index("cz")) * lax.axis_size(
        "cc"
    ) + lax.axis_index("cc")
    row_index = lax.axis_index("rz") * lax.axis_size("ry") + lax.axis_index("ry")
    n_col = lax.axis_size("cx") * lax.axis_size("cz") * lax.axis_size("cc")
    panels_per_row = n_col // (lax.axis_size("rz") * lax.axis_size("ry"))
    my_rows = lax.dynamic_slice_in_dim(neighbours, row_index * row_blocks, row_blocks, 0)
    own_cols = lax.dynamic_slice_in_dim(my_rows, col_index * slot_count, slot_count, 1) - col_index * CB

    roots = (col_index == panels)[:, None, None]
    stacked = jnp.where(roots, density[None], jnp.zeros((), density.dtype))
    bands = []
    for s in range(2):
        number = panels[s]
        offset = number % panels_per_row * CB * BLK
        band = lax.dynamic_slice_in_dim(density, offset, CB * BLK, 0)
        bands.append(jnp.where(row_index == number // panels_per_row, band, jnp.zeros_like(band)))

    stacked = stacked.reshape(2 * density.shape[0], density.shape[1])
    part = lax.psum_scatter(stacked, COL_AXES, scatter_dimension=0, tiled=True)

    band_all = jnp.stack(bands)
    owner_row = panels // panels_per_row
    n_ry = lax.axis_size("ry")
    band_all = row_broadcast(band_all, owner_row // n_ry, owner_row % n_ry)
    part, band_all = lax.optimization_barrier((part, band_all))
    left_all = lax.all_gather(part, COL_AXES, axis=0, tiled=True).reshape(2, *density.shape)

    left_tables = []
    right_tables = []
    for s in range(2):
        number = panels[s]
        group_cols = lax.dynamic_slice_in_dim(my_rows, number * slot_count, slot_count, 1) - number * CB
        left_tables.append(group_cols.reshape(-1))
        band_rows = lax.dynamic_slice_in_dim(neighbours, number * CB, CB, 0)
        band_cols = lax.dynamic_slice_in_dim(band_rows, col_index * slot_count, slot_count, 1) - col_index * CB
        right_tables.append(band_cols.reshape(-1))
    right_dense = place(band_all, jnp.concatenate(right_tables), slot_count, CB, 768, True)
    table = jnp.concatenate(left_tables + [own_cols.reshape(-1)])
    return fused_product(left_all, right_dense, table, slot_count, 256)


def solution(mesh):
    n_row, n_col = mesh.devices.shape
    sub = Mesh(mesh.devices.reshape(2, n_row // 2, 4, n_col // 8, 2), ROW_AXES + COL_AXES)
    return jax.shard_map(
        on_device,
        mesh=sub,
        in_specs=(P(ROW_AXES, COL_AXES), P(), P()),
        out_specs=P(ROW_AXES, COL_AXES),
        check_vma=False,
    )
```

```python
import functools

import jax
import jax.numpy as jnp
from jax import lax
from jax.experimental import pallas as pl
from jax.experimental.pallas import tpu as pltpu
from jax.sharding import Mesh
from jax.sharding import PartitionSpec as P

BLK = 64
CB = 12
ROW_AXES = ("rz", "ry")
COL_AXES = ("cx", "cz", "cc")


def _halves(chunk):
    return chunk, pltpu.roll(chunk, BLK, 1)


def _place_kernel(src_blocks, dst_blocks, tile_rows, block_rows, table, values, out):
    _place_body(src_blocks, dst_blocks, tile_rows, block_rows, table, values, out, pl.program_id(0), pl.program_id(1), 0)


def _place_body(src_blocks, dst_blocks, tile_rows, block_rows, table, values, out, step, tile, offset):
    lanes = lax.broadcasted_iota(jnp.int32, (BLK, 2 * BLK), 1)
    high = lanes >= BLK
    half = lanes // BLK
    placing = src_blocks < dst_blocks
    entries = src_blocks if placing else dst_blocks
    per_step = block_rows * entries

    def one_row(q, carry):
        base = offset + step * per_step + (tile * (tile_rows // BLK) + q) * entries
        rows = pl.ds(pl.multiple_of(q * BLK, BLK), BLK)
        plain = []
        swapped = []
        for c in range(src_blocks // 2):
            a, b = _halves(values[0, rows, pl.ds(c * 2 * BLK, 2 * BLK)])
            plain.append(a)
            swapped.append(b)
        sources = []
        for t in range(src_blocks):
            own = plain[t // 2]
            other = swapped[t // 2]
            if t % 2 == 0:
                sources.append(jnp.where(high, other, own))
            else:
                sources.append(jnp.where(high, own, other))
        for p in range(dst_blocks // 2):
            acc = jnp.zeros((BLK, 2 * BLK), out.dtype)
            for t in range(src_blocks):
                if placing:
                    hit = half + 2 * p == table[base + t]
                else:
                    hit = jnp.where(high, table[base + 2 * p + 1], table[base + 2 * p]) == t
                acc = jnp.where(hit, sources[t], acc)
            out[rows, pl.ds(p * 2 * BLK, 2 * BLK)] = acc
        return carry

    lax.fori_loop(0, tile_rows // BLK, one_row, 0)


def _fused_kernel(tile_rows, block_rows, slots, table, left, right, out, dense, product):
    tile = pl.program_id(1)
    steps = left.shape[0]
    width = CB * BLK
    for s in range(steps):
        view = dense.at[:, pl.ds(s * width, width)]
        _place_body(slots, CB, tile_rows, block_rows, table, left.at[pl.ds(s, 1)], view, s, tile, 0)
    product[0] = jnp.dot(dense[...], right[...], preferred_element_type=jnp.float32).astype(product.dtype)
    _place_body(CB, slots, tile_rows, block_rows, table, product, out, 0, tile, steps * block_rows * slots)


def fused_product(left, right, table, slots, tile_rows):
    steps, rows, _ = left.shape
    return pl.pallas_call(
        functools.partial(_fused_kernel, tile_rows, rows // BLK, slots),
        out_shape=jax.ShapeDtypeStruct((rows, slots * BLK), left.dtype),
        grid_spec=pltpu.PrefetchScalarGridSpec(
            num_scalar_prefetch=1,
            grid=(1, rows // tile_rows),
            in_specs=[
                pl.BlockSpec((steps, tile_rows, left.shape[2]), lambda s, g, tab: (0, g, 0)),
                pl.BlockSpec(right.shape, lambda s, g, tab: (0, 0)),
            ],
            out_specs=pl.BlockSpec((tile_rows, slots * BLK), lambda s, g, tab: (g, 0)),
            scratch_shapes=[
                pltpu.VMEM((tile_rows, steps * CB * BLK), left.dtype),
                pltpu.VMEM((1, tile_rows, right.shape[1]), left.dtype),
            ],
        ),
    )(table, left, right)


def place(values, table, src_blocks, dst_blocks, tile_rows, by_rows):
    steps, rows, _ = values.shape
    tiles = rows // tile_rows
    if not by_rows:
        out_shape = (rows, steps * dst_blocks * BLK)
        out_map = lambda s, g, tab: (g, s)
    else:
        out_shape = (steps * rows, dst_blocks * BLK)
        out_map = lambda s, g, tab: (s * tiles + g, 0)
    return pl.pallas_call(
        functools.partial(_place_kernel, src_blocks, dst_blocks, tile_rows, rows // BLK),
        out_shape=jax.ShapeDtypeStruct(out_shape, values.dtype),
        grid_spec=pltpu.PrefetchScalarGridSpec(
            num_scalar_prefetch=1,
            grid=(steps, tiles),
            in_specs=[pl.BlockSpec((1, tile_rows, src_blocks * BLK), lambda s, g, tab: (s, g, 0))],
            out_specs=pl.BlockSpec((tile_rows, dst_blocks * BLK), out_map),
        ),
    )(table, values)


def ring_shift(x, axis, size, step):
    return lax.ppermute(x, axis, [(i, (i + step) % size) for i in range(size)])


def row_broadcast(buf, root_z, root_y):
    z = lax.axis_index("rz")
    y = lax.axis_index("ry")
    ny = lax.axis_size("ry")
    got = ring_shift(buf, "rz", 2, 1)
    buf = jnp.where((z == root_z)[:, None, None], buf, got)
    dist = ((y - root_y + ny) % ny)[:, None, None]
    from_left = ring_shift(buf, "ry", ny, 1)
    from_right = ring_shift(buf, "ry", ny, -1)
    buf = jnp.where(dist == 1, from_left, jnp.where(dist == ny - 1, from_right, buf))
    half = buf.shape[1] // 2
    first = ring_shift(buf[:, :half], "ry", ny, 1)
    second = ring_shift(buf[:, half:], "ry", ny, -1)
    far = jnp.concatenate([first, second], axis=1)
    return jnp.where(dist == 2, far, buf)


def on_device(density, neighbours, panels):
    row_blocks = density.shape[0] // BLK
    slot_count = density.shape[1] // BLK
    col_index = (lax.axis_index("cx") * lax.axis_size("cz") + lax.axis_index("cz")) * lax.axis_size(
        "cc"
    ) + lax.axis_index("cc")
    row_index = lax.axis_index("rz") * lax.axis_size("ry") + lax.axis_index("ry")
    n_col = lax.axis_size("cx") * lax.axis_size("cz") * lax.axis_size("cc")
    panels_per_row = n_col // (lax.axis_size("rz") * lax.axis_size("ry"))
    my_rows = lax.dynamic_slice_in_dim(neighbours, row_index * row_blocks, row_blocks, 0)
    own_cols = lax.dynamic_slice_in_dim(my_rows, col_index * slot_count, slot_count, 1) - col_index * CB

    roots = (col_index == panels)[:, None, None]
    stacked = jnp.where(roots, density[None], jnp.zeros((), density.dtype))
    bands = []
    for s in range(2):
        number = panels[s]
        offset = number % panels_per_row * CB * BLK
        band = lax.dynamic_slice_in_dim(density, offset, CB * BLK, 0)
        bands.append(jnp.where(row_index == number // panels_per_row, band, jnp.zeros_like(band)))

    stacked = stacked.reshape(2 * density.shape[0], density.shape[1])
    part = lax.psum_scatter(stacked, COL_AXES, scatter_dimension=0, tiled=True)

    band_all = jnp.stack(bands)
    owner_row = panels // panels_per_row
    n_ry = lax.axis_size("ry")
    band_all = row_broadcast(band_all, owner_row // n_ry, owner_row % n_ry)
    part, band_all = lax.optimization_barrier((part, band_all))
    left_all = lax.all_gather(part, COL_AXES, axis=0, tiled=True).reshape(2, *density.shape)

    left_tables = []
    right_tables = []
    for s in range(2):
        number = panels[s]
        group_cols = lax.dynamic_slice_in_dim(my_rows, number * slot_count, slot_count, 1) - number * CB
        left_tables.append(group_cols.reshape(-1))
        band_rows = lax.dynamic_slice_in_dim(neighbours, number * CB, CB, 0)
        band_cols = lax.dynamic_slice_in_dim(band_rows, col_index * slot_count, slot_count, 1) - col_index * CB
        right_tables.append(band_cols.reshape(-1))
    right_dense = place(band_all, jnp.concatenate(right_tables), slot_count, CB, 768, True)
    table = jnp.concatenate(left_tables + [own_cols.reshape(-1)])
    return fused_product(left_all, right_dense, table, slot_count, 512)


def solution(mesh):
    n_row, n_col = mesh.devices.shape
    sub = Mesh(mesh.devices.reshape(2, n_row // 2, 4, n_col // 8, 2), ROW_AXES + COL_AXES)
    return jax.shard_map(
        on_device,
        mesh=sub,
        in_specs=(P(ROW_AXES, COL_AXES), P(), P()),
        out_specs=P(ROW_AXES, COL_AXES),
        check_vma=False,
    )
```
